128 devices in a mesh: win: 16 (over y, x), tile: 8 (over z, core).
Axes of the slice: x: 4, y: 4, z: 4, core: 2. Of those that a mesh axis runs over, the one named last changes fastest.
Arguments:
- spectra: bfloat16 [768, 16, 128, 128], P('win', 'tile'), may hold values from -20 to 20
- segment_ids: int32 [768], P('win'), may hold values from 0 to 95, never falling along the last dimension, each value on 1 to 16 neighbouring positions
- pair_blocks: int32 [24, 2], P('tile'), may hold values from 0 to 15, as said below
- pair_count: int32 [8], P('tile'), may hold values from 2 to 3
Outputs:
- correlations: float32 [24, 128, 64, 128], P('tile', 'win')
The draws below stay inside these ranges and needn't reach their ends.
Inputs may be any that keep to these rules, and one draw needn't show every extreme that they name: `pair_blocks`: slot r of owner t = r // 3 names blocks a and b with |a - b| <= 2, both among the blocks (t - 1) * 2 to (t + 2) * 2 - 1; every slot holds valid blocks, live or not. `segment_ids`: segment numbers never fall along the windows; each segment spans 1 to 16 windows.
All inputs are finite; a program needn't handle non-finite values.
Results may differ from the reference program's by a relative error of at most 0.00065.
Values may be sent and summed in bfloat16 or wider, within the bound.
No kernel may reach another device: no remote copies, remote signals or barrier semaphores. Data moves between devices by JAX's collectives and lax.ppermute only.
A program may use at most 192 MiB of HBM per device.

```python
import math
import jax
import jax.numpy as jnp
import numpy as np
from jax import lax

BC = 128
FB = 64
SUB = 32
NFFT = 4096
F0 = 64
LAGS = 64
BLK_DEV = 2
PMAX = 3
SEG_MOST = 16
WIN = 768
NB = 16
SEGS = 96
N_TILE = 8


def draw_spectra(key, part):
    first_key, second_key = jax.random.split(jax.random.fold_in(key, 11), 2)
    shape = (WIN, NB, BC, 2 * FB)
    base = jnp.clip(jax.random.normal(first_key, shape, jnp.float32), -6.0, 6.0)
    rough = jnp.exp(jax.random.uniform(second_key, shape, jnp.float32, -1.2, 1.2))
    return (base * rough).astype(jnp.bfloat16)


def draw_pair_blocks(key, part):
    total = N_TILE * PMAX
    rows = jnp.arange(total, dtype=jnp.int32)
    owner = rows // PMAX
    slot = rows % PMAX
    lowest = owner * BLK_DEV
    first_key, second_key, third_key = jax.random.split(jax.random.fold_in(key, 23), 3)
    offset = jax.random.randint(first_key, (total,), 0, BLK_DEV, dtype=jnp.int32)
    stride = jax.random.randint(second_key, (total,), 0, BLK_DEV + 1, dtype=jnp.int32)
    either_side = jax.random.randint(third_key, (total,), -BLK_DEV, BLK_DEV + 1, dtype=jnp.int32)
    lower_first = lowest - BLK_DEV + offset
    lower_second = lower_first + stride
    upper_second = lowest + BLK_DEV + offset
    upper_first = upper_second - stride
    own_first = lowest + offset
    own_second = own_first + either_side
    first = jnp.where(slot == 0, lower_first, jnp.where(slot == 1, upper_first, own_first))
    second = jnp.where(slot == 0, lower_second, jnp.where(slot == 1, upper_second, own_second))
    first = jnp.clip(first, 0, NB - 1)
    second = jnp.clip(second, 0, NB - 1)
    return jnp.stack([first, second], axis=1).astype(jnp.int32)


def draw_pair_count(key, part):
    first_key, second_key = jax.random.split(jax.random.fold_in(key, 37))
    base = jax.random.randint(first_key, (N_TILE,), 2, PMAX + 1, dtype=jnp.int32)
    chosen = jax.random.randint(second_key, (), 0, N_TILE, dtype=jnp.int32)
    return jnp.where(jnp.arange(N_TILE, dtype=jnp.int32) == chosen, PMAX, base).astype(jnp.int32)


def profile(number_of, total, limit, lean):
    weights = [(1 << 20) // math.isqrt(grade ** lean) + 1 for grade in range(2, number_of + 1)]
    surplus, holding = total - limit - (number_of - 1), [1] * (number_of - 1)
    while surplus > 0:
        candidates = [i for i in range(number_of - 1) if holding[i] < limit]
        pool, remaining = sum([weights[i] for i in candidates]), surplus
        for i in candidates:
            extra = min(limit - holding[i], max(1, remaining * weights[i] // pool), surplus)
            holding[i] = holding[i] + extra
            surplus = surplus - extra
    return np.array([limit] + holding)


def uneven_parts(key, count, total, reach, slope):
    if count == 2:
        one = jax.random.randint(key, (), max(1, total - reach), min(reach, total - 1) + 1)
        return jnp.stack([one, total - one])
    sizes = jnp.asarray(profile(count, total, reach, slope), jnp.int32)
    twos = (count - 1) // 2
    giver, receiver = sizes[1:1 + 2 * twos:2], sizes[2:2 + 2 * twos:2]
    slack = jnp.minimum(giver - 1, reach - receiver)
    passed = jax.random.randint(jax.random.fold_in(key, 1), (twos,), 0, 1 << 20) % (slack + 1)
    sizes = sizes.at[1:1 + 2 * twos:2].set(giver - passed).at[2:2 + 2 * twos:2].set(receiver + passed)
    return sizes[jax.random.permutation(jax.random.fold_in(key, 2), count)]


def setup_inputs(seed: int = 0) -> dict:
    key_list = jax.random.split(jax.random.key(seed), 5)
    return {
        "spectra": draw_spectra(jax.random.fold_in(key_list[4], 71), 0),
        "segment_ids": jnp.searchsorted(jnp.cumsum(uneven_parts(key_list[1], SEGS, WIN, SEG_MOST, 2)), jnp.arange(WIN), side="right").astype(jnp.int32),
        "pair_blocks": draw_pair_blocks(jax.random.fold_in(key_list[4], 71), 0),
        "pair_count": draw_pair_count(jax.random.fold_in(key_list[4], 71), 0),
    }


def whiten(spectra):
    values = spectra.astype(jnp.float32)
    real_part = values[..., :FB]
    imag_part = values[..., FB:]
    power_sum = real_part * real_part + imag_part * imag_part
    band_power = lax.optimization_barrier(jnp.mean(power_sum.reshape(power_sum.shape[:-1] + (FB // SUB, SUB)), axis=-1)) + 1e-06
    scales = jnp.repeat(1.0 / jnp.sqrt(band_power), SUB, axis=-1)
    both_scales = jnp.concatenate([scales, scales], axis=-1)
    return (values * both_scales).astype(jnp.bfloat16)

def window_weights(segment_ids, segment_total):
    one_hot = (segment_ids[:, None] == jnp.arange(segment_total, dtype=jnp.int32)[None, :]).astype(jnp.float32)
    sizes = lax.optimization_barrier(jnp.sum(one_hot, axis=0))
    return 1.0 / jnp.dot(one_hot, sizes, precision=lax.Precision.HIGHEST)

def lag_table():
    bins = jnp.arange(FB, dtype=jnp.int32) + F0
    shifts = jnp.arange(LAGS, dtype=jnp.int32) - LAGS // 2
    products = jnp.mod(bins[:, None] * shifts[None, :], NFFT)
    phases = products.astype(jnp.float32) * (2.0 * math.pi / NFFT)
    norm_scale = 1.0 / math.sqrt(FB)
    return jnp.concatenate([jnp.cos(phases), -jnp.sin(phases)], axis=0) * norm_scale

def cross_spectrum(first_block, second_block, weight):
    left = (first_block.astype(jnp.float32) * weight[:, None, None]).astype(jnp.bfloat16)
    left_real, left_imag = (left[..., :FB], left[..., FB:])
    right_real, right_imag = (second_block[..., :FB], second_block[..., FB:])
    left_both = jnp.stack([jnp.stack([left_real, left_imag]), jnp.stack([left_imag, -left_real])]).astype(jnp.float32)
    right_both = jnp.stack([right_real, right_imag]).astype(jnp.float32)
    cross = jnp.einsum('qpwcf,pwdf->cqfd', left_both, right_both, precision=lax.Precision.HIGHEST)
    return cross.reshape(cross.shape[0], 2 * FB, cross.shape[3])

def reference(spectra, segment_ids, pair_blocks, pair_count):
    whitened = whiten(spectra)
    weight = window_weights(segment_ids, SEGS)
    basis = lag_table()

    def one_slot(slot_index):
        first_block = lax.dynamic_index_in_dim(whitened, pair_blocks[slot_index, 0], 1, keepdims=False)
        second_block = lax.dynamic_index_in_dim(whitened, pair_blocks[slot_index, 1], 1, keepdims=False)
        spectrum = cross_spectrum(first_block, second_block, weight)
        lagged = jnp.einsum('cgd,gl->cld', spectrum, basis, precision=lax.Precision.HIGHEST)
        live_flag = (slot_index % PMAX < pair_count[slot_index // PMAX]).astype(jnp.float32)
        return lagged * live_flag
    return lax.map(one_slot, jnp.arange(N_TILE * PMAX, dtype=jnp.int32))
```

```python
import math

import jax
import jax.numpy as jnp
from jax import lax
from jax.sharding import PartitionSpec as P

FB = 64
SUB = 32
NFFT = 4096
F0 = 64
LAGS = 64
SEG_MOST = 16


def padded(value, sides, width):
    for axis, dim in sides:
        count, length = (lax.axis_size(axis), value.shape[dim])
        up = [(i, (i + 1) % count) for i in range(count - 1)]
        down = [(j, i) for i, j in up]
        last = lax.slice_in_dim(value, length - width, length, axis=dim)
        initial = lax.slice_in_dim(value, 0, width, axis=dim)
        before = lax.ppermute(last, axis, up)
        after = lax.ppermute(initial, axis, down)
        value = jnp.concatenate([before, value, after], axis=dim)
    return value


def whiten(spectra):
    values = spectra.astype(jnp.float32)
    real_part = values[..., :FB]
    imag_part = values[..., FB:]
    power_sum = real_part * real_part + imag_part * imag_part
    band_power = (
        jnp.mean(power_sum.reshape(power_sum.shape[:-1] + (FB // SUB, SUB)), axis=-1) + 1e-06
    )
    scales = jnp.repeat(1.0 / jnp.sqrt(band_power), SUB, axis=-1)
    both_scales = jnp.concatenate([scales, scales], axis=-1)
    return (values * both_scales).astype(jnp.bfloat16)


def lag_table():
    bins = jnp.arange(FB, dtype=jnp.int32) + F0
    shifts = jnp.arange(LAGS, dtype=jnp.int32) - LAGS // 2
    products = jnp.mod(bins[:, None] * shifts[None, :], NFFT)
    phases = products.astype(jnp.float32) * (2.0 * math.pi / NFFT)
    norm_scale = 1.0 / math.sqrt(FB)
    return jnp.concatenate([jnp.cos(phases), -jnp.sin(phases)], axis=0) * norm_scale


def window_weight(segment_ids):
    count = lax.axis_size("win")
    length = segment_ids.shape[0]
    up = [(i, i + 1) for i in range(count - 1)]
    down = [(j, i) for i, j in up]
    shifted = segment_ids + 1
    before = lax.ppermute(shifted[length - SEG_MOST:], "win", up) - 1
    after = lax.ppermute(shifted[:SEG_MOST], "win", down) - 1
    extended = jnp.concatenate([before, segment_ids, after])
    same = (segment_ids[:, None] == extended[None, :]).astype(jnp.float32)
    sizes = jnp.sum(same, axis=1)
    return 1.0 / sizes


def slot_corr(first_block, second_block, weight, basis):
    left = (first_block.astype(jnp.float32) * weight[:, None, None]).astype(jnp.bfloat16)
    left_real, left_imag = (left[..., :FB], left[..., FB:])
    right_real, right_imag = (second_block[..., :FB], second_block[..., FB:])
    left_both = jnp.stack([jnp.stack([left_real, left_imag]), jnp.stack([left_imag, -left_real])])
    right_both = jnp.stack([right_real, right_imag])
    cross = jnp.einsum(
        "qpwcf,pwdf->cqfd", left_both, right_both, preferred_element_type=jnp.float32
    )
    cross = cross.reshape(cross.shape[0], 2 * FB, cross.shape[3])
    return jnp.einsum("cgd,gl->cld", cross, basis, precision=lax.Precision.HIGHEST)


def on_device(spectra, segment_ids, pair_blocks, pair_count):
    whitened = whiten(spectra)
    weight = window_weight(segment_ids)
    block_count = whitened.shape[1]
    extended = padded(whitened, (("tile", 1),), block_count)
    first_local = lax.axis_index("tile") * block_count - block_count
    basis = lag_table()
    slot_total = pair_blocks.shape[0]
    live_count = pair_count[0]
    win_count = lax.axis_size("win")

    def one_slot(slot_index):
        first_block = lax.dynamic_index_in_dim(
            extended, pair_blocks[slot_index, 0] - first_local, 1, keepdims=False
        )
        second_block = lax.dynamic_index_in_dim(
            extended, pair_blocks[slot_index, 1] - first_local, 1, keepdims=False
        )
        corr = slot_corr(first_block, second_block, weight, basis)
        live = (slot_index < live_count).astype(jnp.float32)
        return corr * live

    slot_numbers = jnp.arange(slot_total, dtype=jnp.int32)
    stacked = jax.vmap(one_slot)(slot_numbers)
    channels = stacked.shape[1]
    grouped = stacked.reshape(slot_total, win_count, channels // win_count, LAGS, -1)
    grouped = jnp.moveaxis(grouped, 1, 0)
    return lax.psum_scatter(grouped, "win", scatter_dimension=0, tiled=False)


def solution(mesh):
    return jax.shard_map(
        on_device,
        mesh=mesh,
        in_specs=(P("win", "tile", None, None), P("win"), P("tile", None), P("tile")),
        out_specs=P("tile", "win", None, None),
        check_vma=False,
    )
```

```python
import functools
import math

import jax
import jax.numpy as jnp
from jax import lax
from jax.experimental import pallas as pl
from jax.experimental.pallas import tpu as pltpu
from jax.sharding import PartitionSpec as P

FB = 64
SUB = 32
NFFT = 4096
F0 = 64
LAGS = 64
SEG_MOST = 16


def padded(value, sides, width):
    for axis, dim in sides:
        count, length = (lax.axis_size(axis), value.shape[dim])
        up = [(i, (i + 1) % count) for i in range(count - 1)]
        down = [(j, i) for i, j in up]
        last = lax.slice_in_dim(value, length - width, length, axis=dim)
        initial = lax.slice_in_dim(value, 0, width, axis=dim)
        before = lax.ppermute(last, axis, up)
        after = lax.ppermute(initial, axis, down)
        value = jnp.concatenate([before, value, after], axis=dim)
    return value


def whiten_transposed(spectra):
    values = spectra.astype(jnp.float32)
    real_part = values[..., :FB]
    imag_part = values[..., FB:]
    power_sum = real_part * real_part + imag_part * imag_part
    band_power = (
        jnp.mean(power_sum.reshape(power_sum.shape[:-1] + (FB // SUB, SUB)), axis=-1) + 1e-06
    )
    scales = jnp.repeat(1.0 / jnp.sqrt(band_power), SUB, axis=-1)
    both_scales = jnp.concatenate([scales, scales], axis=-1)
    whitened = (values * both_scales).astype(jnp.bfloat16)
    return jnp.transpose(whitened, (1, 3, 0, 2))


def lag_table():
    bins = jnp.arange(FB, dtype=jnp.int32) + F0
    shifts = jnp.arange(LAGS, dtype=jnp.int32) - LAGS // 2
    products = jnp.mod(bins[:, None] * shifts[None, :], NFFT)
    phases = products.astype(jnp.float32) * (2.0 * math.pi / NFFT)
    norm_scale = 1.0 / math.sqrt(FB)
    return jnp.concatenate([jnp.cos(phases), -jnp.sin(phases)], axis=0) * norm_scale


def window_weight(segment_ids):
    count = lax.axis_size("win")
    length = segment_ids.shape[0]
    up = [(i, i + 1) for i in range(count - 1)]
    down = [(j, i) for i, j in up]
    shifted = segment_ids + 1
    before = lax.ppermute(shifted[length - SEG_MOST:], "win", up) - 1
    after = lax.ppermute(shifted[:SEG_MOST], "win", down) - 1
    extended = jnp.concatenate([before, segment_ids, after])
    same = (segment_ids[:, None] == extended[None, :]).astype(jnp.float32)
    sizes = jnp.sum(same, axis=1)
    return 1.0 / sizes


def corr_kernel(index_ref, a_ref, b_ref, w_ref, basis_ref, o_ref, x_ref, *, groups):
    channels = a_ref.shape[2]
    weight = w_ref[...]
    dims = (((0,), (0,)), ((), ()))

    def cross_step(k, carry):
        a_real = (a_ref[k].astype(jnp.float32) * weight).astype(jnp.bfloat16)
        a_imag = (a_ref[k + FB].astype(jnp.float32) * weight).astype(jnp.bfloat16)
        right = jnp.concatenate([b_ref[k], b_ref[k + FB]], axis=0)
        first = jnp.concatenate([a_real, a_imag], axis=0)
        second = jnp.concatenate([a_imag, -a_real], axis=0)
        base = pl.multiple_of(k * 2 * channels, 2 * channels)
        x_ref[pl.ds(base, channels), :] = lax.dot_general(
            first, right, dims, preferred_element_type=jnp.float32
        )
        x_ref[pl.ds(base + channels, channels), :] = lax.dot_general(
            second, right, dims, preferred_element_type=jnp.float32
        )
        return carry

    lax.fori_loop(0, FB, cross_step, 0)
    live = (index_ref[2] > 0).astype(jnp.float32)
    basis = basis_ref[...]
    rows = channels // groups

    def lag_step(c, carry):
        real_rows = x_ref[pl.ds(c, FB, stride=2 * channels), :]
        imag_rows = x_ref[pl.ds(c + channels, FB, stride=2 * channels), :]
        both = jnp.concatenate([real_rows, imag_rows], axis=0)
        lagged = jnp.dot(
            basis, both, precision=lax.Precision.HIGHEST, preferred_element_type=jnp.float32
        )
        o_ref[c // rows, c % rows] = lagged * live
        return carry

    lax.fori_loop(0, channels, lag_step, 0)


def slot_corr(index, extended, weight, basis_t, groups):
    blocks, bins, windows, channels = extended.shape
    kernel = functools.partial(corr_kernel, groups=groups)
    spec = pl.BlockSpec((None, bins, windows, channels), lambda i, ref: (ref[0], 0, 0, 0))
    second_spec = pl.BlockSpec((None, bins, windows, channels), lambda i, ref: (ref[1], 0, 0, 0))
    grid_spec = pltpu.PrefetchScalarGridSpec(
        num_scalar_prefetch=1,
        grid=(1,),
        in_specs=[
            spec,
            second_spec,
            pl.BlockSpec((windows, 1), lambda i, ref: (0, 0)),
            pl.BlockSpec((LAGS, 2 * FB), lambda i, ref: (0, 0)),
        ],
        out_specs=pl.BlockSpec(
            (groups, channels // groups, LAGS, channels), lambda i, ref: (0, 0, 0, 0)
        ),
        scratch_shapes=[pltpu.VMEM((FB * 2 * channels, channels), jnp.float32)],
    )
    return pl.pallas_call(
        kernel,
        grid_spec=grid_spec,
        out_shape=jax.ShapeDtypeStruct(
            (groups, channels // groups, LAGS, channels), jnp.float32
        ),
        compiler_params=pltpu.CompilerParams(vmem_limit_bytes=48 * 1024 * 1024),
    )(index, extended, extended, weight[:, None], basis_t)


def on_device(spectra, segment_ids, pair_blocks, pair_count):
    weight = window_weight(segment_ids)
    whitened = whiten_transposed(spectra)
    block_count = whitened.shape[0]
    extended = padded(whitened, (("tile", 0),), block_count)
    first_local = lax.axis_index("tile") * block_count - block_count
    basis_t = jnp.transpose(lag_table())
    slot_total = pair_blocks.shape[0]
    live_count = pair_count[0]
    win_count = lax.axis_size("win")
    local = jnp.clip(pair_blocks - first_local, 0, extended.shape[0] - 1)

    shares = []
    for slot in range(slot_total):
        index = jnp.stack(
            [local[slot, 0], local[slot, 1], (slot < live_count).astype(jnp.int32)]
        )
        corr = slot_corr(index, extended, weight, basis_t, win_count)
        shares.append(lax.psum_scatter(corr, "win", scatter_dimension=0, tiled=False))
    return jnp.stack(shares)


def solution(mesh):
    return jax.shard_map(
        on_device,
        mesh=mesh,
        in_specs=(P("win", "tile", None, None), P("win"), P("tile", None), P("tile")),
        out_specs=P("tile", "win", None, None),
        check_vma=False,
    )
```

```python
import math
import jax
import jax.numpy as jnp
from jax import lax
from jax.experimental.layout import Layout, with_layout_constraint
from jax.sharding import PartitionSpec as P

FB = 64
SUB = 32
NFFT = 4096
F0 = 64
LAGS = 64
SEG_MOST = 16


def padded(value, sides, width):
    for axis, dim in sides:
        count, length = (lax.axis_size(axis), value.shape[dim])
        up = [(i, (i + 1) % count) for i in range(count - 1)]
        down = [(j, i) for i, j in up]
        last = lax.slice_in_dim(value, length - width, length, axis=dim)
        initial = lax.slice_in_dim(value, 0, width, axis=dim)
        before = lax.ppermute(last, axis, up)
        after = lax.ppermute(initial, axis, down)
        value = jnp.concatenate([before, value, after], axis=dim)
    return value


def whiten_transposed(spectra):
    values = spectra.astype(jnp.float32)
    real_part = values[..., :FB]
    imag_part = values[..., FB:]
    power_sum = real_part * real_part + imag_part * imag_part
    band_power = (
        jnp.mean(power_sum.reshape(power_sum.shape[:-1] + (FB // SUB, SUB)), axis=-1) + 1e-06
    )
    scales = jnp.repeat(1.0 / jnp.sqrt(band_power), SUB, axis=-1)
    both_scales = jnp.concatenate([scales, scales], axis=-1)
    whitened = (values * both_scales).astype(jnp.bfloat16)
    return jnp.transpose(whitened, (1, 3, 0, 2))


def lag_table():
    bins = jnp.arange(FB, dtype=jnp.int32) + F0
    shifts = jnp.arange(LAGS, dtype=jnp.int32) - LAGS // 2
    products = jnp.mod(bins[:, None] * shifts[None, :], NFFT)
    phases = products.astype(jnp.float32) * (2.0 * math.pi / NFFT)
    norm_scale = 1.0 / math.sqrt(FB)
    return jnp.concatenate([jnp.cos(phases), -jnp.sin(phases)], axis=0) * norm_scale


def window_weight(segment_ids):
    count = lax.axis_size("win")
    length = segment_ids.shape[0]
    up = [(i, i + 1) for i in range(count - 1)]
    down = [(j, i) for i, j in up]
    shifted = segment_ids + 1
    before = lax.ppermute(shifted[length - SEG_MOST:], "win", up) - 1
    after = lax.ppermute(shifted[:SEG_MOST], "win", down) - 1
    extended = jnp.concatenate([before, segment_ids, after])
    same = (segment_ids[:, None] == extended[None, :]).astype(jnp.float32)
    sizes = jnp.sum(same, axis=1)
    return 1.0 / sizes


def on_device(spectra, segment_ids, pair_blocks, pair_count):
    weight = window_weight(segment_ids)
    whitened = whiten_transposed(spectra)
    block_count = whitened.shape[0]
    extended = padded(whitened, (("tile", 0),), block_count)
    first_local = lax.axis_index("tile") * block_count - block_count
    basis = lag_table().reshape(2, FB, LAGS)
    slot_total = pair_blocks.shape[0]
    live_count = pair_count[0]
    win_count = lax.axis_size("win")
    local = jnp.clip(pair_blocks - first_local, 0, extended.shape[0] - 1)
    first = jnp.take(extended, local[:, 0], axis=0)
    second = jnp.take(extended, local[:, 1], axis=0)
    left = (first.astype(jnp.float32) * weight[None, None, :, None]).astype(jnp.bfloat16)
    left_real, left_imag = (left[:, :FB], left[:, FB:])
    right_real, right_imag = (second[:, :FB], second[:, FB:])
    left_both = jnp.stack([jnp.stack([left_real, left_imag]), jnp.stack([left_imag, -left_real])])
    right_both = jnp.stack([right_real, right_imag])
    cross = jnp.einsum(
        "qpskwc,pskwd->skqcd", left_both, right_both, preferred_element_type=jnp.float32
    )
    live = (jnp.arange(slot_total) < live_count).astype(jnp.float32)
    channels = cross.shape[3]
    cross = cross.reshape(slot_total, FB, 2, win_count, channels // win_count, channels)
    corr = jnp.einsum(
        "skqgcd,qkl->gsc" + "ld", cross, basis, precision=lax.Precision.HIGHEST
    )
    corr = corr * live[None, :, None, None, None]
    corr = with_layout_constraint(corr, Layout((0, 1, 2, 3, 4)))
    return lax.psum_scatter(corr, "win", scatter_dimension=0, tiled=False)


def solution(mesh):
    return jax.shard_map(
        on_device,
        mesh=mesh,
        in_specs=(P("win", "tile", None, None), P("win"), P("tile", None), P("tile")),
        out_specs=P("tile", "win", None, None),
        check_vma=False,
    )
```

```python
import math
import jax
import jax.numpy as jnp
from jax import lax
from jax.experimental.layout import Layout, with_layout_constraint
from jax.sharding import PartitionSpec as P

FB = 64
SUB = 32
NFFT = 4096
F0 = 64
LAGS = 64
SEG_MOST = 16


def padded(value, sides, width):
    for axis, dim in sides:
        count, length = (lax.axis_size(axis), value.shape[dim])
        up = [(i, (i + 1) % count) for i in range(count - 1)]
        down = [(j, i) for i, j in up]
        last = lax.slice_in_dim(value, length - width, length, axis=dim)
        initial = lax.slice_in_dim(value, 0, width, axis=dim)
        before = lax.ppermute(last, axis, up)
        after = lax.ppermute(initial, axis, down)
        value = jnp.concatenate([before, value, after], axis=dim)
    return value


def whiten_transposed(spectra):
    values = spectra.astype(jnp.float32)
    real_part = values[..., :FB]
    imag_part = values[..., FB:]
    power_sum = real_part * real_part + imag_part * imag_part
    band_power = (
        jnp.mean(power_sum.reshape(power_sum.shape[:-1] + (FB // SUB, SUB)), axis=-1) + 1e-06
    )
    scales = jnp.repeat(1.0 / jnp.sqrt(band_power), SUB, axis=-1)
    both_scales = jnp.concatenate([scales, scales], axis=-1)
    whitened = (values * both_scales).astype(jnp.bfloat16)
    return jnp.transpose(whitened, (1, 3, 0, 2))


def lag_table():
    bins = jnp.arange(FB, dtype=jnp.int32) + F0
    shifts = jnp.arange(LAGS, dtype=jnp.int32) - LAGS // 2
    products = jnp.mod(bins[:, None] * shifts[None, :], NFFT)
    phases = products.astype(jnp.float32) * (2.0 * math.pi / NFFT)
    norm_scale = 1.0 / math.sqrt(FB)
    return jnp.concatenate([jnp.cos(phases), -jnp.sin(phases)], axis=0) * norm_scale


def window_weight(segment_ids):
    count = lax.axis_size("win")
    length = segment_ids.shape[0]
    up = [(i, i + 1) for i in range(count - 1)]
    down = [(j, i) for i, j in up]
    shifted = segment_ids + 1
    before = lax.ppermute(shifted[length - SEG_MOST:], "win", up) - 1
    after = lax.ppermute(shifted[:SEG_MOST], "win", down) - 1
    extended = jnp.concatenate([before, segment_ids, after])
    same = (segment_ids[:, None] == extended[None, :]).astype(jnp.float32)
    sizes = jnp.sum(same, axis=1)
    return 1.0 / sizes


def on_device(spectra, segment_ids, pair_blocks, pair_count):
    weight = window_weight(segment_ids)
    whitened = whiten_transposed(spectra)
    block_count = whitened.shape[0]
    extended = padded(whitened, (("tile", 0),), block_count)
    first_local = lax.axis_index("tile") * block_count - block_count
    basis = lag_table().reshape(2, FB, LAGS)
    slot_total = pair_blocks.shape[0]
    live_count = pair_count[0]
    win_count = lax.axis_size("win")
    local = jnp.clip(pair_blocks - first_local, 0, extended.shape[0] - 1)
    first = jnp.take(extended, local[:, 0], axis=0)
    second = jnp.take(extended, local[:, 1], axis=0)
    left = (first.astype(jnp.float32) * weight[None, None, :, None]).astype(jnp.bfloat16)
    left_real, left_imag = (left[:, :FB], left[:, FB:])
    right_real, right_imag = (second[:, :FB], second[:, FB:])
    left_both = jnp.stack([jnp.stack([left_real, left_imag]), jnp.stack([left_imag, -left_real])])
    right_both = jnp.stack([right_real, right_imag])
    cross = jnp.einsum(
        "qpskwc,pskwd->skqcd", left_both, right_both, preferred_element_type=jnp.float32
    )
    live = (jnp.arange(slot_total) < live_count).astype(jnp.float32)
    channels = cross.shape[3]
    cross = cross.reshape(slot_total, FB, 2, win_count, channels // win_count, channels)
    corr = jnp.einsum(
        "skqgcd,qkl->gscld", cross, basis, precision=lax.Precision.HIGH
    )
    corr = corr * live[None, :, None, None, None]
    corr = with_layout_constraint(corr, Layout((0, 1, 2, 3, 4)))
    return lax.psum_scatter(corr, "win", scatter_dimension=0, tiled=False)


def solution(mesh):
    return jax.shard_map(
        on_device,
        mesh=mesh,
        in_specs=(P("win", "tile", None, None), P("win"), P("tile", None), P("tile")),
        out_specs=P("tile", "win", None, None),
        check_vma=False,
    )
```

```python
import math
import jax
import jax.numpy as jnp
from jax import lax
from jax.experimental.layout import Layout, with_layout_constraint
from jax.sharding import PartitionSpec as P

FB = 64
SUB = 32
NFFT = 4096
F0 = 64
LAGS = 64
SEG_MOST = 16


def padded(value, sides, width):
    for axis, dim in sides:
        count, length = (lax.axis_size(axis), value.shape[dim])
        up = [(i, (i + 1) % count) for i in range(count - 1)]
        down = [(j, i) for i, j in up]
        last = lax.slice_in_dim(value, length - width, length, axis=dim)
        initial = lax.slice_in_dim(value, 0, width, axis=dim)
        before = lax.ppermute(last, axis, up)
        after = lax.ppermute(initial, axis, down)
        value = jnp.concatenate([before, value, after], axis=dim)
    return value


def whiten_transposed(spectra):
    values = spectra.astype(jnp.float32)
    real_part = values[..., :FB]
    imag_part = values[..., FB:]
    power_sum = real_part * real_part + imag_part * imag_part
    band_power = (
        jnp.mean(power_sum.reshape(power_sum.shape[:-1] + (FB // SUB, SUB)), axis=-1) + 1e-06
    )
    scales = jnp.repeat(1.0 / jnp.sqrt(band_power), SUB, axis=-1)
    both_scales = jnp.concatenate([scales, scales], axis=-1)
    whitened = (values * both_scales).astype(jnp.bfloat16)
    return jnp.transpose(whitened, (1, 3, 0, 2))


def lag_table():
    bins = jnp.arange(FB, dtype=jnp.int32) + F0
    shifts = jnp.arange(LAGS, dtype=jnp.int32) - LAGS // 2
    products = jnp.mod(bins[:, None] * shifts[None, :], NFFT)
    phases = products.astype(jnp.float32) * (2.0 * math.pi / NFFT)
    norm_scale = 1.0 / math.sqrt(FB)
    return jnp.concatenate([jnp.cos(phases), -jnp.sin(phases)], axis=0) * norm_scale


def window_weight(segment_ids):
    count = lax.axis_size("win")
    length = segment_ids.shape[0]
    up = [(i, i + 1) for i in range(count - 1)]
    down = [(j, i) for i, j in up]
    shifted = segment_ids + 1
    before = lax.ppermute(shifted[length - SEG_MOST:], "win", up) - 1
    after = lax.ppermute(shifted[:SEG_MOST], "win", down) - 1
    extended = jnp.concatenate([before, segment_ids, after])
    same = (segment_ids[:, None] == extended[None, :]).astype(jnp.float32)
    sizes = jnp.sum(same, axis=1)
    return 1.0 / sizes


def on_device(spectra, segment_ids, pair_blocks, pair_count):
    weight = window_weight(segment_ids)
    whitened = whiten_transposed(spectra)
    block_count = whitened.shape[0]
    extended = padded(whitened, (("tile", 0),), block_count)
    first_local = lax.axis_index("tile") * block_count - block_count
    basis = lag_table().reshape(2, FB, LAGS)
    slot_total = pair_blocks.shape[0]
    live_count = pair_count[0]
    win_count = lax.axis_size("win")
    local = jnp.clip(pair_blocks - first_local, 0, extended.shape[0] - 1)
    first = jnp.stack(
        [lax.dynamic_index_in_dim(extended, local[i, 0], 0, False) for i in range(slot_total)]
    )
    second = jnp.stack(
        [lax.dynamic_index_in_dim(extended, local[i, 1], 0, False) for i in range(slot_total)]
    )
    left = (first.astype(jnp.float32) * weight[None, None, :, None]).astype(jnp.bfloat16)
    left_real, left_imag = (left[:, :FB], left[:, FB:])
    right_real, right_imag = (second[:, :FB], second[:, FB:])
    left_both = jnp.stack([jnp.stack([left_real, left_imag]), jnp.stack([left_imag, -left_real])])
    right_both = jnp.stack([right_real, right_imag])
    cross = jnp.einsum(
        "qpskwc,pskwd->skqcd", left_both, right_both, preferred_element_type=jnp.float32
    )
    live = (jnp.arange(slot_total) < live_count).astype(jnp.float32)
    channels = cross.shape[3]
    cross = cross.reshape(slot_total, FB, 2, win_count, channels // win_count, channels)
    corr = jnp.einsum(
        "skqgcd,qkl->gscld", cross, basis, precision=lax.Precision.HIGH
    )
    corr = corr * live[None, :, None, None, None]
    corr = with_layout_constraint(corr, Layout((0, 1, 2, 3, 4)))
    return lax.psum_scatter(corr, "win", scatter_dimension=0, tiled=False)


def solution(mesh):
    return jax.shard_map(
        on_device,
        mesh=mesh,
        in_specs=(P("win", "tile", None, None), P("win"), P("tile", None), P("tile")),
        out_specs=P("tile", "win", None, None),
        check_vma=False,
    )
```

```python
import math
import jax
import jax.numpy as jnp
from jax import lax
from jax.experimental.layout import Layout, with_layout_constraint
from jax.sharding import PartitionSpec as P

FB = 64
SUB = 32
NFFT = 4096
F0 = 64
LAGS = 64
SEG_MOST = 16


def padded(value, sides, width):
    for axis, dim in sides:
        count, length = (lax.axis_size(axis), value.shape[dim])
        up = [(i, (i + 1) % count) for i in range(count - 1)]
        down = [(j, i) for i, j in up]
        last = lax.slice_in_dim(value, length - width, length, axis=dim)
        initial = lax.slice_in_dim(value, 0, width, axis=dim)
        before = lax.ppermute(last, axis, up)
        after = lax.ppermute(initial, axis, down)
        value = jnp.concatenate([before, value, after], axis=dim)
    return value


def whiten_transposed(spectra):
    values = spectra.astype(jnp.float32)
    real_part = values[..., :FB]
    imag_part = values[..., FB:]
    power_sum = real_part * real_part + imag_part * imag_part
    band_power = (
        jnp.mean(power_sum.reshape(power_sum.shape[:-1] + (FB // SUB, SUB)), axis=-1) + 1e-06
    )
    scales = jnp.repeat(1.0 / jnp.sqrt(band_power), SUB, axis=-1)
    both_scales = jnp.concatenate([scales, scales], axis=-1)
    whitened = (values * both_scales).astype(jnp.bfloat16)
    return jnp.transpose(whitened, (1, 3, 0, 2))


def lag_table():
    bins = jnp.arange(FB, dtype=jnp.int32) + F0
    shifts = jnp.arange(LAGS, dtype=jnp.int32) - LAGS // 2
    products = jnp.mod(bins[:, None] * shifts[None, :], NFFT)
    phases = products.astype(jnp.float32) * (2.0 * math.pi / NFFT)
    norm_scale = 1.0 / math.sqrt(FB)
    return jnp.concatenate([jnp.cos(phases), -jnp.sin(phases)], axis=0) * norm_scale


def window_weight(segment_ids):
    count = lax.axis_size("win")
    length = segment_ids.shape[0]
    up = [(i, i + 1) for i in range(count - 1)]
    down = [(j, i) for i, j in up]
    shifted = segment_ids + 1
    before = lax.ppermute(shifted[length - SEG_MOST:], "win", up) - 1
    after = lax.ppermute(shifted[:SEG_MOST], "win", down) - 1
    extended = jnp.concatenate([before, segment_ids, after])
    same = (segment_ids[:, None] == extended[None, :]).astype(jnp.float32)
    sizes = jnp.sum(same, axis=1)
    return 1.0 / sizes


def on_device(spectra, segment_ids, pair_blocks, pair_count):
    weight = window_weight(segment_ids)
    block_count = spectra.shape[1]
    pieces = [whiten_transposed(spectra[:, i : i + 1]) for i in range(block_count)]
    count = lax.axis_size("tile")
    up = [(i, i + 1) for i in range(count - 1)]
    down = [(j, i) for i, j in up]
    before = [lax.ppermute(piece, "tile", up) for piece in pieces]
    after = [lax.ppermute(piece, "tile", down) for piece in pieces]
    extended = jnp.concatenate(before + pieces + after, axis=0)
    first_local = lax.axis_index("tile") * block_count - block_count
    basis = lag_table().reshape(2, FB, LAGS)
    slot_total = pair_blocks.shape[0]
    live_count = pair_count[0]
    win_count = lax.axis_size("win")
    local = jnp.clip(pair_blocks - first_local, 0, extended.shape[0] - 1)
    first = jnp.stack(
        [lax.dynamic_index_in_dim(extended, local[i, 0], 0, False) for i in range(slot_total)]
    )
    second = jnp.stack(
        [lax.dynamic_index_in_dim(extended, local[i, 1], 0, False) for i in range(slot_total)]
    )
    left = (first.astype(jnp.float32) * weight[None, None, :, None]).astype(jnp.bfloat16)
    left_real, left_imag = (left[:, :FB], left[:, FB:])
    right_real, right_imag = (second[:, :FB], second[:, FB:])
    left_both = jnp.stack([jnp.stack([left_real, left_imag]), jnp.stack([left_imag, -left_real])])
    right_both = jnp.stack([right_real, right_imag])
    cross = jnp.einsum(
        "qpskwc,pskwd->skqcd", left_both, right_both, preferred_element_type=jnp.float32
    )
    live = (jnp.arange(slot_total) < live_count).astype(jnp.float32)
    channels = cross.shape[3]
    cross = cross.reshape(slot_total, FB, 2, win_count, channels // win_count, channels)
    corr = jnp.einsum(
        "skqgcd,qkl->gscld", cross, basis, precision=lax.Precision.HIGH
    )
    corr = corr * live[None, :, None, None, None]
    corr = with_layout_constraint(corr, Layout((0, 1, 2, 3, 4)))
    return lax.psum_scatter(corr, "win", scatter_dimension=0, tiled=False)


def solution(mesh):
    return jax.shard_map(
        on_device,
        mesh=mesh,
        in_specs=(P("win", "tile", None, None), P("win"), P("tile", None), P("tile")),
        out_specs=P("tile", "win", None, None),
        check_vma=False,
    )
```

```python
import math
import jax
import jax.numpy as jnp
from jax import lax
from jax.experimental.layout import Layout, with_layout_constraint
from jax.sharding import PartitionSpec as P

FB = 64
SUB = 32
NFFT = 4096
F0 = 64
LAGS = 64
SEG_MOST = 16


def padded(value, sides, width):
    for axis, dim in sides:
        count, length = (lax.axis_size(axis), value.shape[dim])
        up = [(i, (i + 1) % count) for i in range(count - 1)]
        down = [(j, i) for i, j in up]
        last = lax.slice_in_dim(value, length - width, length, axis=dim)
        initial = lax.slice_in_dim(value, 0, width, axis=dim)
        before = lax.ppermute(last, axis, up)
        after = lax.ppermute(initial, axis, down)
        value = jnp.concatenate([before, value, after], axis=dim)
    return value


def whiten_transposed(spectra):
    values = spectra.astype(jnp.float32)
    real_part = values[..., :FB]
    imag_part = values[..., FB:]
    power_sum = real_part * real_part + imag_part * imag_part
    band_power = (
        jnp.mean(power_sum.reshape(power_sum.shape[:-1] + (FB // SUB, SUB)), axis=-1) + 1e-06
    )
    scales = jnp.repeat(1.0 / jnp.sqrt(band_power), SUB, axis=-1)
    both_scales = jnp.concatenate([scales, scales], axis=-1)
    whitened = (values * both_scales).astype(jnp.bfloat16)
    return jnp.transpose(whitened, (1, 3, 0, 2))


def lag_table():
    bins = jnp.arange(FB, dtype=jnp.int32) + F0
    shifts = jnp.arange(LAGS, dtype=jnp.int32) - LAGS // 2
    products = jnp.mod(bins[:, None] * shifts[None, :], NFFT)
    phases = products.astype(jnp.float32) * (2.0 * math.pi / NFFT)
    norm_scale = 1.0 / math.sqrt(FB)
    return jnp.concatenate([jnp.cos(phases), -jnp.sin(phases)], axis=0) * norm_scale


def window_weight(segment_ids):
    count = lax.axis_size("win")
    length = segment_ids.shape[0]
    up = [(i, i + 1) for i in range(count - 1)]
    down = [(j, i) for i, j in up]
    shifted = segment_ids + 1
    before = lax.ppermute(shifted[length - SEG_MOST:], "win", up) - 1
    after = lax.ppermute(shifted[:SEG_MOST], "win", down) - 1
    extended = jnp.concatenate([before, segment_ids, after])
    same = (segment_ids[:, None] == extended[None, :]).astype(jnp.float32)
    sizes = jnp.sum(same, axis=1)
    return 1.0 / sizes


def on_device(spectra, segment_ids, pair_blocks, pair_count):
    weight = window_weight(segment_ids)
    spectra, weight = lax.optimization_barrier((spectra, weight))
    block_count = spectra.shape[1]
    pieces = [whiten_transposed(spectra[:, i : i + 1]) for i in range(block_count)]
    count = lax.axis_size("tile")
    up = [(i, i + 1) for i in range(count - 1)]
    down = [(j, i) for i, j in up]
    before = [lax.ppermute(piece, "tile", up) for piece in pieces]
    after = [lax.ppermute(piece, "tile", down) for piece in pieces]
    extended = jnp.concatenate(before + pieces + after, axis=0)
    first_local = lax.axis_index("tile") * block_count - block_count
    basis = lag_table().reshape(2, FB, LAGS)
    slot_total = pair_blocks.shape[0]
    live_count = pair_count[0]
    win_count = lax.axis_size("win")
    local = jnp.clip(pair_blocks - first_local, 0, extended.shape[0] - 1)
    first = jnp.stack(
        [lax.dynamic_index_in_dim(extended, local[i, 0], 0, False) for i in range(slot_total)]
    )
    second = jnp.stack(
        [lax.dynamic_index_in_dim(extended, local[i, 1], 0, False) for i in range(slot_total)]
    )
    left = (first.astype(jnp.float32) * weight[None, None, :, None]).astype(jnp.bfloat16)
    left_real, left_imag = (left[:, :FB], left[:, FB:])
    right_real, right_imag = (second[:, :FB], second[:, FB:])
    left_both = jnp.stack([jnp.stack([left_real, left_imag]), jnp.stack([left_imag, -left_real])])
    right_both = jnp.stack([right_real, right_imag])
    cross = jnp.einsum(
        "qpskwc,pskwd->skqcd", left_both, right_both, preferred_element_type=jnp.float32
    )
    live = (jnp.arange(slot_total) < live_count).astype(jnp.float32)
    channels = cross.shape[3]
    cross = cross.reshape(slot_total, FB, 2, win_count, channels // win_count, channels)
    corr = jnp.einsum(
        "skqgcd,qkl->gscld", cross, basis, precision=lax.Precision.HIGH
    )
    corr = corr * live[None, :, None, None, None]
    corr = with_layout_constraint(corr, Layout((0, 1, 2, 3, 4)))
    return lax.psum_scatter(corr, "win", scatter_dimension=0, tiled=False)


def solution(mesh):
    return jax.shard_map(
        on_device,
        mesh=mesh,
        in_specs=(P("win", "tile", None, None), P("win"), P("tile", None), P("tile")),
        out_specs=P("tile", "win", None, None),
        check_vma=False,
    )
```

```python
import math
import jax
import jax.numpy as jnp
from jax import lax
from jax.experimental.layout import Layout, with_layout_constraint
from jax.sharding import PartitionSpec as P

FB = 64
SUB = 32
NFFT = 4096
F0 = 64
LAGS = 64
SEG_MOST = 16


def padded(value, sides, width):
    for axis, dim in sides:
        count, length = (lax.axis_size(axis), value.shape[dim])
        up = [(i, (i + 1) % count) for i in range(count - 1)]
        down = [(j, i) for i, j in up]
        last = lax.slice_in_dim(value, length - width, length, axis=dim)
        initial = lax.slice_in_dim(value, 0, width, axis=dim)
        before = lax.ppermute(last, axis, up)
        after = lax.ppermute(initial, axis, down)
        value = jnp.concatenate([before, value, after], axis=dim)
    return value


def whiten_transposed(spectra):
    values = spectra.astype(jnp.float32)
    real_part = values[..., :FB]
    imag_part = values[..., FB:]
    power_sum = real_part * real_part + imag_part * imag_part
    band_power = (
        jnp.mean(power_sum.reshape(power_sum.shape[:-1] + (FB // SUB, SUB)), axis=-1) + 1e-06
    )
    scales = jnp.repeat(1.0 / jnp.sqrt(band_power), SUB, axis=-1)
    both_scales = jnp.concatenate([scales, scales], axis=-1)
    whitened = (values * both_scales).astype(jnp.bfloat16)
    return jnp.transpose(whitened, (1, 3, 0, 2))


def lag_table():
    bins = jnp.arange(FB, dtype=jnp.int32) + F0
    shifts = jnp.arange(LAGS, dtype=jnp.int32) - LAGS // 2
    products = jnp.mod(bins[:, None] * shifts[None, :], NFFT)
    phases = products.astype(jnp.float32) * (2.0 * math.pi / NFFT)
    norm_scale = 1.0 / math.sqrt(FB)
    return jnp.concatenate([jnp.cos(phases), -jnp.sin(phases)], axis=0) * norm_scale


def window_weight(segment_ids):
    count = lax.axis_size("win")
    length = segment_ids.shape[0]
    up = [(i, i + 1) for i in range(count - 1)]
    down = [(j, i) for i, j in up]
    shifted = segment_ids + 1
    before = lax.ppermute(shifted[length - SEG_MOST:], "win", up) - 1
    after = lax.ppermute(shifted[:SEG_MOST], "win", down) - 1
    extended = jnp.concatenate([before, segment_ids, after])
    same = (segment_ids[:, None] == extended[None, :]).astype(jnp.float32)
    sizes = jnp.sum(same, axis=1)
    return 1.0 / sizes


def on_device(spectra, segment_ids, pair_blocks, pair_count):
    weight = window_weight(segment_ids)
    block_count = spectra.shape[1]
    count = lax.axis_size("tile")
    up = [(i, i + 1) for i in range(count - 1)]
    down = [(j, i) for i, j in up]
    raw = spectra[:, 0:1]
    raw_before = lax.ppermute(raw, "tile", up)
    raw_after = lax.ppermute(raw, "tile", down)
    pieces = [whiten_transposed(spectra[:, i : i + 1]) for i in range(block_count)]
    before = [whiten_transposed(raw_before)] + [
        lax.ppermute(piece, "tile", up) for piece in pieces[1:]
    ]
    after = [whiten_transposed(raw_after)] + [
        lax.ppermute(piece, "tile", down) for piece in pieces[1:]
    ]
    extended = jnp.concatenate(before + pieces + after, axis=0)
    first_local = lax.axis_index("tile") * block_count - block_count
    basis = lag_table().reshape(2, FB, LAGS)
    slot_total = pair_blocks.shape[0]
    live_count = pair_count[0]
    win_count = lax.axis_size("win")
    local = jnp.clip(pair_blocks - first_local, 0, extended.shape[0] - 1)
    first = jnp.stack(
        [lax.dynamic_index_in_dim(extended, local[i, 0], 0, False) for i in range(slot_total)]
    )
    second = jnp.stack(
        [lax.dynamic_index_in_dim(extended, local[i, 1], 0, False) for i in range(slot_total)]
    )
    left = (first.astype(jnp.float32) * weight[None, None, :, None]).astype(jnp.bfloat16)
    left_real, left_imag = (left[:, :FB], left[:, FB:])
    right_real, right_imag = (second[:, :FB], second[:, FB:])
    left_both = jnp.stack([jnp.stack([left_real, left_imag]), jnp.stack([left_imag, -left_real])])
    right_both = jnp.stack([right_real, right_imag])
    cross = jnp.einsum(
        "qpskwc,pskwd->skqcd", left_both, right_both, preferred_element_type=jnp.float32
    )
    live = (jnp.arange(slot_total) < live_count).astype(jnp.float32)
    channels = cross.shape[3]
    cross = cross.reshape(slot_total, FB, 2, win_count, channels // win_count, channels)
    corr = jnp.einsum(
        "skqgcd,qkl->gscld", cross, basis, precision=lax.Precision.HIGH
    )
    corr = corr * live[None, :, None, None, None]
    corr = with_layout_constraint(corr, Layout((0, 1, 2, 3, 4)))
    return lax.psum_scatter(corr, "win", scatter_dimension=0, tiled=False)


def solution(mesh):
    return jax.shard_map(
        on_device,
        mesh=mesh,
        in_specs=(P("win", "tile", None, None), P("win"), P("tile", None), P("tile")),
        out_specs=P("tile", "win", None, None),
        check_vma=False,
    )
```

```python
import math
import jax
import jax.numpy as jnp
from jax import lax
from jax.experimental.layout import Layout, with_layout_constraint
from jax.sharding import PartitionSpec as P

FB = 64
SUB = 32
NFFT = 4096
F0 = 64
LAGS = 64
SEG_MOST = 16


def padded(value, sides, width):
    for axis, dim in sides:
        count, length = (lax.axis_size(axis), value.shape[dim])
        up = [(i, (i + 1) % count) for i in range(count - 1)]
        down = [(j, i) for i, j in up]
        last = lax.slice_in_dim(value, length - width, length, axis=dim)
        initial = lax.slice_in_dim(value, 0, width, axis=dim)
        before = lax.ppermute(last, axis, up)
        after = lax.ppermute(initial, axis, down)
        value = jnp.concatenate([before, value, after], axis=dim)
    return value


def whiten_transposed(spectra):
    values = spectra.astype(jnp.float32)
    real_part = values[..., :FB]
    imag_part = values[..., FB:]
    power_sum = real_part * real_part + imag_part * imag_part
    band_power = (
        jnp.mean(power_sum.reshape(power_sum.shape[:-1] + (FB // SUB, SUB)), axis=-1) + 1e-06
    )
    scales = jnp.repeat(1.0 / jnp.sqrt(band_power), SUB, axis=-1)
    both_scales = jnp.concatenate([scales, scales], axis=-1)
    whitened = (values * both_scales).astype(jnp.bfloat16)
    return jnp.transpose(whitened, (1, 3, 0, 2))


def lag_table():
    bins = jnp.arange(FB, dtype=jnp.int32) + F0
    shifts = jnp.arange(LAGS, dtype=jnp.int32) - LAGS // 2
    products = jnp.mod(bins[:, None] * shifts[None, :], NFFT)
    phases = products.astype(jnp.float32) * (2.0 * math.pi / NFFT)
    norm_scale = 1.0 / math.sqrt(FB)
    return jnp.concatenate([jnp.cos(phases), -jnp.sin(phases)], axis=0) * norm_scale


def window_weight(segment_ids):
    count = lax.axis_size("win")
    length = segment_ids.shape[0]
    up = [(i, i + 1) for i in range(count - 1)]
    down = [(j, i) for i, j in up]
    shifted = segment_ids + 1
    before = lax.ppermute(shifted[length - SEG_MOST:], "win", up) - 1
    after = lax.ppermute(shifted[:SEG_MOST], "win", down) - 1
    extended = jnp.concatenate([before, segment_ids, after])
    same = (segment_ids[:, None] == extended[None, :]).astype(jnp.float32)
    sizes = jnp.sum(same, axis=1)
    return 1.0 / sizes


def on_device(spectra, segment_ids, pair_blocks, pair_count):
    weight = window_weight(segment_ids)
    block_count = spectra.shape[1]
    blocks = [spectra[:, i : i + 1] for i in range(block_count)]
    blocks[1], weight = lax.optimization_barrier((blocks[1], weight))
    pieces = [whiten_transposed(block) for block in blocks]
    count = lax.axis_size("tile")
    up = [(i, i + 1) for i in range(count - 1)]
    down = [(j, i) for i, j in up]
    before = [lax.ppermute(piece, "tile", up) for piece in pieces]
    after = [lax.ppermute(piece, "tile", down) for piece in pieces]
    extended = jnp.concatenate(before + pieces + after, axis=0)
    first_local = lax.axis_index("tile") * block_count - block_count
    basis = lag_table().reshape(2, FB, LAGS)
    slot_total = pair_blocks.shape[0]
    live_count = pair_count[0]
    win_count = lax.axis_size("win")
    local = jnp.clip(pair_blocks - first_local, 0, extended.shape[0] - 1)
    first = jnp.stack(
        [lax.dynamic_index_in_dim(extended, local[i, 0], 0, False) for i in range(slot_total)]
    )
    second = jnp.stack(
        [lax.dynamic_index_in_dim(extended, local[i, 1], 0, False) for i in range(slot_total)]
    )
    left = (first.astype(jnp.float32) * weight[None, None, :, None]).astype(jnp.bfloat16)
    left_real, left_imag = (left[:, :FB], left[:, FB:])
    right_real, right_imag = (second[:, :FB], second[:, FB:])
    left_both = jnp.stack([jnp.stack([left_real, left_imag]), jnp.stack([left_imag, -left_real])])
    right_both = jnp.stack([right_real, right_imag])
    cross = jnp.einsum(
        "qpskwc,pskwd->skqcd", left_both, right_both, preferred_element_type=jnp.float32
    )
    live = (jnp.arange(slot_total) < live_count).astype(jnp.float32)
    channels = cross.shape[3]
    cross = cross.reshape(slot_total, FB, 2, win_count, channels // win_count, channels)
    corr = jnp.einsum(
        "skqgcd,qkl->gscld", cross, basis, precision=lax.Precision.HIGH
    )
    corr = corr * live[None, :, None, None, None]
    corr = with_layout_constraint(corr, Layout((0, 1, 2, 3, 4)))
    return lax.psum_scatter(corr, "win", scatter_dimension=0, tiled=False)


def solution(mesh):
    return jax.shard_map(
        on_device,
        mesh=mesh,
        in_specs=(P("win", "tile", None, None), P("win"), P("tile", None), P("tile")),
        out_specs=P("tile", "win", None, None),
        check_vma=False,
    )
```
